32 devices in a mesh: cfg: 2 (over x), tm: 4 (over z), height: 4 (over y, core).
Axes of the slice: x: 2, y: 2, z: 4, core: 2. Of those that a mesh axis runs over, the one named last changes fastest.
Arguments:
- query: bfloat16 [2, 4, 4, 1, 384, 1536], P('cfg', 'tm', 'height'), may hold values from -6.5 to 6.5
- keyval: bfloat16 [2, 2, 4, 4, 1, 384, 1536], P(None, 'cfg', 'tm', 'height'), may hold values from -6.5 to 6.5
- hidden: bfloat16 [2, 4, 4, 1, 384, 3072], P('cfg', 'tm', 'height'), may hold values from -3 to 3
- out_weight: bfloat16 [1536, 3072], replicated, may hold values from -0.15625 to 0.15625
- gate_scale: float32 [2, 3072], P('cfg'), may hold values from 0.5 to 2
- guidance: float32 [1], replicated, may hold values from 1.5 to 4
- counts: int32 [4, 4, 1], replicated, may hold values from 192 to 384, as said below
Outputs:
- guided: bfloat16 [4, 4, 1, 384, 3072], P('tm', 'height', None, None, 'cfg')
The draws below stay inside these ranges and needn't reach their ends.
Inputs may be any that keep to these rules, and one draw needn't show every extreme that they name: `counts`: A tile's valid tokens are its first ones; every tile outside the last time tile and the last height tile has 384.
All inputs are finite; a program needn't handle non-finite values.
Results may differ from the reference program's by a relative error of at most 0.011.
Values may be sent and summed in bfloat16 or wider, within the bound.
No kernel may reach another device: no remote copies, remote signals or barrier semaphores. Data moves between devices by JAX's collectives and lax.ppermute only.
A program may use at most 192 MiB of HBM per device.

```python
import math
import jax
import jax.numpy as jnp
from jax import lax

D = 3072
HEADS = 12
HEAD_DIM = 128
TILE = 384
WIDTH_TILES = 1
CHANNELS = 1536
TIME_TILES = 4
HEIGHT_TILES = 4


def draw_query(key, part):
    shape = (2, TIME_TILES, HEIGHT_TILES, WIDTH_TILES, TILE, CHANNELS)
    base = 1.6 * jax.random.truncated_normal(jax.random.fold_in(key, 1), -4.0, 4.0, shape, jnp.float32)
    return base.astype(jnp.bfloat16)


def draw_keyval(key, part):
    shape = (2, 2, TIME_TILES, HEIGHT_TILES, WIDTH_TILES, TILE, CHANNELS)
    base = 1.6 * jax.random.truncated_normal(jax.random.fold_in(key, 2), -4.0, 4.0, shape, jnp.float32)
    return base.astype(jnp.bfloat16)


def draw_counts(key, part):
    shape = (TIME_TILES, HEIGHT_TILES, WIDTH_TILES)
    ragged_values = jax.random.randint(jax.random.fold_in(key, 4), shape, TILE // 2, TILE + 1, jnp.int32)
    time_at = jnp.arange(TIME_TILES, dtype=jnp.int32).reshape(TIME_TILES, 1, 1)
    height_at = jnp.arange(HEIGHT_TILES, dtype=jnp.int32).reshape(1, HEIGHT_TILES, 1)
    ragged = (time_at == TIME_TILES - 1) | (height_at == HEIGHT_TILES - 1)
    return jnp.where(ragged, ragged_values, TILE).astype(jnp.int32)


def block_scale(own_key, shape, cuts, smallest, largest):
    def one(dim, parts):
        steps = jax.random.uniform(jax.random.fold_in(jax.random.fold_in(own_key, 6), dim), (parts,), jnp.float32, smallest / len(cuts), largest / len(cuts))
        return jnp.repeat(jnp.exp(steps), shape[dim] // parts).reshape((-1,) + (1,) * (len(shape) - dim - 1))

    factor_of = one(*cuts[0])
    for cut in cuts[1:]:
        factor_of = factor_of * one(*cut)
    return factor_of


def normal_values(key, dims, spread, limit, shards=(), held_as=jnp.bfloat16):
    array = spread * jax.random.normal(key, dims, jnp.float32)
    if shards:
        array = array * block_scale(key, dims, shards, -0.22, 0.18)
    return jnp.clip(array, -limit, limit).astype(held_as)


def setup_inputs(seed: int = 0) -> dict:
    seeds = jax.random.split(jax.random.key(seed), 8)
    query = draw_query(jax.random.fold_in(seeds[7], 71), 0)
    keyval = draw_keyval(jax.random.fold_in(seeds[7], 71), 0)
    hidden = normal_values(seeds[2], (2, TIME_TILES, HEIGHT_TILES, WIDTH_TILES, TILE, D), 0.5, 3.0, ((0, 2), (1, 4), (2, 4)))
    out_weight = normal_values(seeds[3], (CHANNELS, D), CHANNELS ** -0.5, 0.15625)
    gate_scale = jnp.clip(jnp.exp(math.log(2.0) - 1.3862944 * jax.random.uniform(seeds[4], (2, D), jnp.float32) ** block_scale(seeds[4], (2, D), ((0, 2),), -0.2, 0.2)), 0.5, 2.0)
    guidance = jnp.clip(jax.random.uniform(seeds[5], (1,), jnp.float32, 1.5, 4.0), 1.5, 4.0)
    counts = draw_counts(jax.random.fold_in(seeds[7], 71), 0)
    return {"query": query, "keyval": keyval, "hidden": hidden, "out_weight": out_weight, "gate_scale": gate_scale, "guidance": guidance, "counts": counts}


masked_score = -1.0e30


def attend_tile(query_tile, key_rows, value_rows, key_live, query_live):
    key_count = key_rows.shape[0]
    queries = query_tile.astype(jnp.float32).reshape(TILE, HEADS, HEAD_DIM)
    key_part = key_rows.astype(jnp.float32).reshape(key_count, HEADS, HEAD_DIM)
    value_part = value_rows.astype(jnp.float32).reshape(key_count, HEADS, HEAD_DIM)
    scores = jnp.einsum("qhd,khd->hqk", queries, key_part) * (HEAD_DIM ** -0.5)
    scores = jnp.where(key_live[None, None, :], scores, masked_score)
    row_max = jnp.max(scores, axis=-1, keepdims=True)
    exponent = jnp.exp(scores - row_max)
    probs = (exponent / jnp.sum(exponent, axis=-1, keepdims=True)).astype(jnp.bfloat16)
    mixed = jnp.einsum("hqk,khd->qhd", probs.astype(jnp.float32), value_part)
    mixed = mixed * query_live[:, None, None]
    return mixed.reshape(TILE, HEADS * HEAD_DIM).astype(jnp.bfloat16)


def reference(query, keyval, hidden, out_weight, gate_scale, guidance, counts):
    tiles = TIME_TILES * HEIGHT_TILES * WIDTH_TILES
    span = min(3, WIDTH_TILES)
    flat_query = query.reshape(2 * tiles, TILE, CHANNELS)
    flat_keyval = keyval.reshape(2, 2 * tiles, TILE, CHANNELS)
    padded_counts = jnp.pad(counts, 1)
    position = jnp.arange(TILE, dtype=jnp.int32)
    step_time = jnp.broadcast_to(jnp.arange(3, dtype=jnp.int32)[:, None, None], (3, 3, span)).reshape(-1)
    step_height = jnp.broadcast_to(jnp.arange(3, dtype=jnp.int32)[None, :, None], (3, 3, span)).reshape(-1)
    step_width = jnp.broadcast_to(jnp.arange(span, dtype=jnp.int32)[None, None, :], (3, 3, span)).reshape(-1)

    def one_tile(tile_index):
        branch = tile_index // tiles
        tile_flat = tile_index % tiles
        time_at = tile_flat // (HEIGHT_TILES * WIDTH_TILES)
        height_at = (tile_flat // WIDTH_TILES) % HEIGHT_TILES
        width_at = tile_flat % WIDTH_TILES
        width_start = jnp.clip(width_at - 1, 0, WIDTH_TILES - span)
        key_time = time_at + step_time - 1
        key_height = height_at + step_height - 1
        key_width = width_start + step_width
        live_count = padded_counts[key_time + 1, key_height + 1, key_width + 1]
        live_count = jnp.where(jnp.abs(key_width - width_at) <= 1, live_count, 0)
        source = branch * tiles + (jnp.clip(key_time, 0, TIME_TILES - 1) * HEIGHT_TILES
                                   + jnp.clip(key_height, 0, HEIGHT_TILES - 1)) * WIDTH_TILES + key_width
        source = source.astype(jnp.int32)
        key_rows = flat_keyval[0][source].reshape(9 * span * TILE, CHANNELS)
        value_rows = flat_keyval[1][source].reshape(9 * span * TILE, CHANNELS)
        key_live = (position[None, :] < live_count[:, None]).reshape(9 * span * TILE)
        own_count = padded_counts[time_at + 1, height_at + 1, width_at + 1]
        query_live = (position < own_count).astype(jnp.float32)
        return attend_tile(flat_query[tile_index], key_rows, value_rows, key_live, query_live)

    attended = lax.map(one_tile, jnp.arange(2 * tiles, dtype=jnp.int32))
    attended = attended.reshape(2, tiles * TILE, CHANNELS)
    flat_hidden = hidden.reshape(2, tiles * TILE, D)
    predictions = []
    for branch in range(2):
        projected = jnp.dot(attended[branch], out_weight, preferred_element_type=jnp.float32)
        predictions.append((flat_hidden[branch].astype(jnp.float32) + gate_scale[branch][None, :] * projected).astype(jnp.bfloat16))
    cond_pred = predictions[0].astype(jnp.float32)
    uncond_pred = predictions[1].astype(jnp.float32)
    guided = uncond_pred + guidance[0] * (cond_pred - uncond_pred)
    return guided.astype(jnp.bfloat16).reshape(TIME_TILES, HEIGHT_TILES, WIDTH_TILES, TILE, D)
```

```python
import functools

import jax
import jax.numpy as jnp
from jax import lax
from jax.experimental import pallas as pl
from jax.experimental.pallas import tpu as pltpu
from jax.sharding import PartitionSpec as P

HEAD_DIM = 128
HEADS_PER_STEP = 2
masked_score = -1e30


def _stage_kernel(cnt_ref, *refs, groups, tile_rows, first, last, scale):
    q_ref = refs[0]
    pos = 1
    kv_refs = []
    for _ in groups:
        kv_refs.append((refs[pos], refs[pos + 1]))
        pos += 2
    if not first:
        m_in, l_in, acc_in = refs[pos : pos + 3]
        pos += 3
    outs = refs[pos:]
    width = q_ref.shape[1]
    for h in range(width // HEAD_DIM):
        lanes = slice(h * HEAD_DIM, (h + 1) * HEAD_DIM)
        q = q_ref[:, lanes]
        if first:
            m_prev = l_prev = acc_prev = None
        else:
            m_prev = m_in[:, lanes]
            l_prev = l_in[:, lanes]
            acc_prev = acc_in[:, lanes]
        base = 0
        for (k_ref, v_ref), n_tiles in zip(kv_refs, groups):
            keys = k_ref[:, :, lanes].reshape(n_tiles * tile_rows, HEAD_DIM)
            vals = v_ref[:, :, lanes].reshape(n_tiles * tile_rows, HEAD_DIM)
            s = lax.dot_general(
                q, keys, (((1,), (1,)), ((), ())), preferred_element_type=jnp.float32
            )
            s = s * scale
            col = lax.broadcasted_iota(jnp.int32, (1, n_tiles * tile_rows), 1)
            live = None
            for j in range(n_tiles):
                lo = j * tile_rows
                here = (col >= lo) & (col < lo + cnt_ref[base + j])
                live = here if live is None else (live | here)
            base += n_tiles
            s = jnp.where(live, s, masked_score)
            m_cur = jnp.max(s, axis=1, keepdims=True)
            if m_prev is None:
                m_new = jnp.broadcast_to(m_cur, (s.shape[0], HEAD_DIM))
            else:
                m_new = jnp.maximum(m_prev, m_cur)
            p = jnp.exp(s - m_new[:, :1])
            row_sum = jnp.sum(p, axis=1, keepdims=True)
            pv = jnp.dot(p.astype(jnp.bfloat16), vals, preferred_element_type=jnp.float32)
            if m_prev is None:
                l_new = jnp.broadcast_to(row_sum, (s.shape[0], HEAD_DIM))
                acc_new = pv
            else:
                alpha = jnp.exp(m_prev - m_new)
                l_new = alpha * l_prev + row_sum
                acc_new = alpha * acc_prev + pv
            m_prev, l_prev, acc_prev = m_new, l_new, acc_new
        if last:
            rows = lax.broadcasted_iota(jnp.int32, (acc_prev.shape[0], HEAD_DIM), 0)
            out = acc_prev / l_prev
            out = jnp.where(rows < cnt_ref[base], out, 0.0)
            outs[0][:, lanes] = out.astype(outs[0].dtype)
        else:
            outs[0][:, lanes] = m_prev
            outs[1][:, lanes] = l_prev
            outs[2][:, lanes] = acc_prev


def attend_stage(query, kv_groups, counts, state, own_count=None):
    rows, channels = query.shape
    groups = tuple(g.shape[1] for g in kv_groups)
    first = state is None
    last = own_count is not None
    block = HEADS_PER_STEP * HEAD_DIM
    steps = channels // block
    scalars = counts if own_count is None else jnp.concatenate([counts, own_count])
    in_specs = [pl.BlockSpec((rows, block), lambda g, c: (0, g))]
    operands = [query]
    for grp in kv_groups:
        n = grp.shape[1]
        in_specs.append(pl.BlockSpec((None, n, rows, block), lambda g, c: (0, 0, 0, g)))
        in_specs.append(pl.BlockSpec((None, n, rows, block), lambda g, c: (1, 0, 0, g)))
        operands += [grp, grp]
    state_spec = pl.BlockSpec((rows, block), lambda g, c: (0, g))
    if not first:
        in_specs += [state_spec] * 3
        operands += list(state)
    if last:
        out_shape = jax.ShapeDtypeStruct((rows, channels), jnp.bfloat16)
        out_specs = state_spec
    else:
        f32 = jax.ShapeDtypeStruct((rows, channels), jnp.float32)
        out_shape = (f32, f32, f32)
        out_specs = (state_spec, state_spec, state_spec)
    kernel = functools.partial(
        _stage_kernel,
        groups=groups,
        tile_rows=rows,
        first=first,
        last=last,
        scale=HEAD_DIM ** (-0.5),
    )
    return pl.pallas_call(
        kernel,
        out_shape=out_shape,
        grid_spec=pltpu.PrefetchScalarGridSpec(
            num_scalar_prefetch=1,
            grid=(steps,),
            in_specs=in_specs,
            out_specs=out_specs,
        ),
        compiler_params=pltpu.CompilerParams(dimension_semantics=("arbitrary",)),
    )(scalars, *operands)


def shift(x, axis, direction):
    size = lax.axis_size(axis)
    if direction > 0:
        pairs = [(i, i + 1) for i in range(size - 1)]
    else:
        pairs = [(i + 1, i) for i in range(size - 1)]
    return lax.ppermute(x, axis, pairs)


def on_device(query, keyval, hidden, out_weight, gate_scale, guidance, counts):
    width_tiles = query.shape[3]
    assert width_tiles == 1
    tile_rows = query.shape[4]
    channels = query.shape[5]
    model_width = hidden.shape[5]
    own_time = lax.axis_index("tm")
    own_height = lax.axis_index("height")
    slab = jnp.pad(counts[:, :, 0], 1)
    slab = lax.dynamic_slice(slab, (own_time, own_height), (3, 3))

    own_kv = keyval.reshape(2, 1, tile_rows, channels)
    own_queries = query.reshape(tile_rows, channels)
    from_before = shift(own_kv, "tm", +1)
    from_after = shift(own_kv, "tm", -1)
    state = attend_stage(own_queries, [own_kv], slab[1, 1:2], None)
    state = attend_stage(
        own_queries, [from_before, from_after], jnp.stack([slab[0, 1], slab[2, 1]]), state
    )
    column = jnp.concatenate([from_before, own_kv, from_after], axis=1)
    from_below = shift(column, "height", +1)
    from_above = shift(column, "height", -1)
    cnt_below = slab[:, 0]
    cnt_above = slab[:, 2]
    attended = attend_stage(
        own_queries,
        [from_below, from_above],
        jnp.concatenate([cnt_below, cnt_above]),
        state,
        own_count=slab[1, 1:2],
    )
    projected = jnp.dot(attended, out_weight, preferred_element_type=jnp.float32)
    stream = hidden.reshape(tile_rows, model_width).astype(jnp.float32)
    prediction = (stream + gate_scale[0][None, :] * projected).astype(jnp.bfloat16)
    prediction = prediction.reshape(1, 1, 1, 1, tile_rows, model_width)
    both = lax.all_to_all(prediction, "cfg", split_axis=5, concat_axis=0, tiled=True)
    cond_pred = both[0].astype(jnp.float32)
    uncond_pred = both[1].astype(jnp.float32)
    guided = uncond_pred + guidance[0] * (cond_pred - uncond_pred)
    return guided.astype(jnp.bfloat16)


def solution(mesh):
    return jax.shard_map(
        on_device,
        mesh=mesh,
        in_specs=(
            P("cfg", "tm", "height", None, None, None),
            P(None, "cfg", "tm", "height", None, None, None),
            P("cfg", "tm", "height", None, None, None),
            P(),
            P("cfg", None),
            P(),
            P(),
        ),
        out_specs=P("tm", "height", None, None, "cfg"),
        check_vma=False,
    )
```

```python
import functools

import jax
import jax.numpy as jnp
from jax import lax
from jax.experimental import pallas as pl
from jax.experimental.pallas import tpu as pltpu
from jax.sharding import PartitionSpec as P

HEAD_DIM = 128
HEADS_PER_STEP = 2
masked_score = -1e30


def _stage_kernel(cnt_ref, *refs, groups, tile_rows, first, last, scale):
    q_ref = refs[0]
    pos = 1
    kv_refs = []
    for _ in groups:
        kv_refs.append((refs[pos], refs[pos + 1]))
        pos += 2
    if not first:
        m_in, l_in, acc_in = refs[pos : pos + 3]
        pos += 3
    outs = refs[pos:]
    width = q_ref.shape[1]
    for h in range(width // HEAD_DIM):
        lanes = slice(h * HEAD_DIM, (h + 1) * HEAD_DIM)
        q = q_ref[:, lanes]
        if first:
            m_prev = l_prev = acc_prev = None
        else:
            m_prev = m_in[:, lanes]
            l_prev = l_in[:, lanes]
            acc_prev = acc_in[:, lanes]
        base = 0
        for (k_ref, v_ref), n_tiles in zip(kv_refs, groups):
            keys = k_ref[:, :, lanes].reshape(n_tiles * tile_rows, HEAD_DIM)
            vals = v_ref[:, :, lanes].reshape(n_tiles * tile_rows, HEAD_DIM)
            s = lax.dot_general(
                q, keys, (((1,), (1,)), ((), ())), preferred_element_type=jnp.float32
            )
            s = s * scale
            col = lax.broadcasted_iota(jnp.int32, (1, n_tiles * tile_rows), 1)
            live = None
            for j in range(n_tiles):
                lo = j * tile_rows
                here = (col >= lo) & (col < lo + cnt_ref[base + j])
                live = here if live is None else (live | here)
            base += n_tiles
            s = jnp.where(live, s, masked_score)
            m_cur = jnp.max(s, axis=1, keepdims=True)
            if m_prev is None:
                m_new = jnp.broadcast_to(m_cur, (s.shape[0], HEAD_DIM))
            else:
                m_new = jnp.maximum(m_prev, m_cur)
            p = jnp.exp(s - m_new[:, :1])
            row_sum = jnp.sum(p, axis=1, keepdims=True)
            pv = jnp.dot(p.astype(jnp.bfloat16), vals, preferred_element_type=jnp.float32)
            if m_prev is None:
                l_new = jnp.broadcast_to(row_sum, (s.shape[0], HEAD_DIM))
                acc_new = pv
            else:
                alpha = jnp.exp(m_prev - m_new)
                l_new = alpha * l_prev + row_sum
                acc_new = alpha * acc_prev + pv
            m_prev, l_prev, acc_prev = m_new, l_new, acc_new
        if last:
            rows = lax.broadcasted_iota(jnp.int32, (acc_prev.shape[0], HEAD_DIM), 0)
            out = acc_prev / l_prev
            out = jnp.where(rows < cnt_ref[base], out, 0.0)
            outs[0][:, lanes] = out.astype(outs[0].dtype)
        else:
            outs[0][:, lanes] = m_prev
            outs[1][:, lanes] = l_prev
            outs[2][:, lanes] = acc_prev


def attend_stage(query, kv_groups, counts, state, own_count=None):
    rows, channels = query.shape
    groups = tuple(g.shape[1] for g in kv_groups)
    first = state is None
    last = own_count is not None
    block = HEADS_PER_STEP * HEAD_DIM
    steps = channels // block
    scalars = counts if own_count is None else jnp.concatenate([counts, own_count])
    in_specs = [pl.BlockSpec((rows, block), lambda g, c: (0, g))]
    operands = [query]
    for grp in kv_groups:
        n = grp.shape[1]
        in_specs.append(pl.BlockSpec((None, n, rows, block), lambda g, c: (0, 0, 0, g)))
        in_specs.append(pl.BlockSpec((None, n, rows, block), lambda g, c: (1, 0, 0, g)))
        operands += [grp, grp]
    state_spec = pl.BlockSpec((rows, block), lambda g, c: (0, g))
    if not first:
        in_specs += [state_spec] * 3
        operands += list(state)
    if last:
        out_shape = jax.ShapeDtypeStruct((rows, channels), jnp.bfloat16)
        out_specs = state_spec
    else:
        f32 = jax.ShapeDtypeStruct((rows, channels), jnp.float32)
        out_shape = (f32, f32, f32)
        out_specs = (state_spec, state_spec, state_spec)
    kernel = functools.partial(
        _stage_kernel,
        groups=groups,
        tile_rows=rows,
        first=first,
        last=last,
        scale=HEAD_DIM ** (-0.5),
    )
    return pl.pallas_call(
        kernel,
        out_shape=out_shape,
        grid_spec=pltpu.PrefetchScalarGridSpec(
            num_scalar_prefetch=1,
            grid=(steps,),
            in_specs=in_specs,
            out_specs=out_specs,
        ),
        compiler_params=pltpu.CompilerParams(dimension_semantics=("arbitrary",)),
    )(scalars, *operands)


def shift(x, axis, direction):
    size = lax.axis_size(axis)
    if direction > 0:
        pairs = [(i, i + 1) for i in range(size - 1)]
    else:
        pairs = [(i + 1, i) for i in range(size - 1)]
    return lax.ppermute(x, axis, pairs)


def swap(x, axis, offset):
    size = lax.axis_size(axis)
    pairs = []
    for lo in range(offset, size - 1, 2):
        pairs += [(lo, lo + 1), (lo + 1, lo)]
    return lax.ppermute(x, axis, pairs)


def on_device(query, keyval, hidden, out_weight, gate_scale, guidance, counts):
    width_tiles = query.shape[3]
    assert width_tiles == 1
    tile_rows = query.shape[4]
    channels = query.shape[5]
    model_width = hidden.shape[5]
    own_time = lax.axis_index("tm")
    own_height = lax.axis_index("height")
    slab = jnp.pad(counts[:, :, 0], 1)
    slab = lax.dynamic_slice(slab, (own_time, own_height), (3, 3))
    even = own_height % 2 == 0
    cnt_sib = jnp.where(even, slab[:, 2], slab[:, 0])
    cnt_cross = jnp.where(even, slab[:, 0], slab[:, 2])

    own_kv = keyval.reshape(2, 1, tile_rows, channels)
    own_queries = query.reshape(tile_rows, channels)
    sib = swap(own_kv, "height", 0)
    cross = swap(own_kv, "height", 1)
    from_before = shift(own_kv, "tm", +1)
    from_after = shift(own_kv, "tm", -1)
    state = attend_stage(own_queries, [own_kv], slab[1, 1:2], None)
    state = attend_stage(
        own_queries, [sib, cross], jnp.stack([cnt_sib[1], cnt_cross[1]]), state
    )
    time_pair = jnp.concatenate([from_before, from_after], axis=1)
    sib_pair = swap(time_pair, "height", 0)
    cross_before = shift(cross, "tm", +1)
    cross_after = shift(cross, "tm", -1)
    state = attend_stage(
        own_queries, [from_before, from_after], jnp.stack([slab[0, 1], slab[2, 1]]), state
    )
    attended = attend_stage(
        own_queries,
        [sib_pair, cross_before, cross_after],
        jnp.stack([cnt_sib[0], cnt_sib[2], cnt_cross[0], cnt_cross[2]]),
        state,
        own_count=slab[1, 1:2],
    )
    projected = jnp.dot(attended, out_weight, preferred_element_type=jnp.float32)
    stream = hidden.reshape(tile_rows, model_width).astype(jnp.float32)
    prediction = (stream + gate_scale[0][None, :] * projected).astype(jnp.bfloat16)
    half = model_width // 2
    branch = lax.axis_index("cfg")
    mine = lax.dynamic_slice_in_dim(prediction, branch * half, half, axis=1)
    other = lax.dynamic_slice_in_dim(prediction, (1 - branch) * half, half, axis=1)
    received = swap(other, "cfg", 0)
    cond_pred = jnp.where(branch == 0, mine, received).astype(jnp.float32)
    uncond_pred = jnp.where(branch == 0, received, mine).astype(jnp.float32)
    guided = uncond_pred + guidance[0] * (cond_pred - uncond_pred)
    return guided.astype(jnp.bfloat16).reshape(1, 1, 1, tile_rows, half)


def solution(mesh):
    return jax.shard_map(
        on_device,
        mesh=mesh,
        in_specs=(
            P("cfg", "tm", "height", None, None, None),
            P(None, "cfg", "tm", "height", None, None, None),
            P("cfg", "tm", "height", None, None, None),
            P(),
            P("cfg", None),
            P(),
            P(),
        ),
        out_specs=P("tm", "height", None, None, "cfg"),
        check_vma=False,
    )
```
